256 devices in a mesh: row: 32 (over y, z_hi, x), col: 8 (over z_lo, core).
Axes of the slice: x: 4, y: 4, z: 8 (z_hi: 2, z_lo: 4; z = z_hi * 4 + z_lo), core: 2. Of those that a mesh axis runs over, the one named last changes fastest.
Arguments:
- trailing: float32 [2, 32768, 4096], P(None, 'row', 'col'), may hold values from -6 to 6
- panel: float32 [2, 32768, 256], P(None, ('row', 'col')), may hold values from -4 to 4
- diag_inverse: float32 [2, 256, 256], replicated, as said below
Outputs:
- scaled: float32 [2, 32768, 256], P(None, ('row', 'col'))
- updated: float32 [2, 32768, 4096], P(None, 'row', 'col')
The draws below stay inside these ranges and needn't reach their ends.
Inputs may be any that keep to these rules, and one draw needn't show every extreme that they name: diag_inverse is complex-symmetric: each part equals its own transpose.
All inputs are finite; a program needn't handle non-finite values.
Results may differ from the reference program's by a relative error of at most 0.00007.
Values sent between devices are 32-bit elements; how exact they have to be, the bound alone decides.
No kernel may reach another device: no remote copies, remote signals or barrier semaphores. Data moves between devices by JAX's collectives and lax.ppermute only.
A program may use at most 64 MiB of HBM per device.

```python
import math
import jax
import jax.numpy as jnp
from jax import lax

M = 32768
B = 256
W = 4096


def draw_diag_inverse(key, part):
    first = jax.random.fold_in(key, 11)
    second = jax.random.fold_in(key, 12)
    base = jax.random.normal(first, (2, B, B), jnp.float32)
    sym = (base + jnp.swapaxes(base, 1, 2)) * (0.7 / math.sqrt(2.0 * B))
    diag_real = jax.random.uniform(second, (B,), jnp.float32, 0.5, 2.0)
    eye_real = jnp.eye(B, dtype=jnp.float32) * diag_real[None, :]
    return sym + jnp.stack([eye_real, jnp.zeros((B, B), jnp.float32)])


def steps_of(rng, shape, pieces, low, high):
    level = 1.0
    for dim, shards_of in pieces:
        draws = jax.random.uniform(jax.random.fold_in(jax.random.fold_in(rng, 6), dim), (shards_of,), jnp.float32, low / len(pieces), high / len(pieces))
        level = level * jnp.repeat(jnp.exp(draws), shape[dim] // shards_of).reshape((-1,) + (1,) * (len(shape) - 1 - dim))
    return level


def gaussian(rng, extent, deviation, reach, cuts=(), held_as=jnp.bfloat16):
    array = deviation * jax.random.normal(rng, extent, jnp.float32)
    if cuts:
        array = array * steps_of(rng, extent, cuts, -0.22, 0.18)
    return jnp.clip(array, -reach, reach).astype(held_as)


def setup_inputs(seed: int = 0) -> dict:
    splits = jax.random.split(jax.random.key(seed), 4)
    return {
        "trailing": gaussian(splits[0], (2, M, W), 1.0, 6.0, ((1, 32), (2, 8)), jnp.float32),
        "panel": gaussian(splits[1], (2, M, B), 0.25, 4.0, ((1, 256),), jnp.float32),
        "diag_inverse": draw_diag_inverse(jax.random.fold_in(splits[3], 71), 0),
    }


def complex_product(left, right):
    hp = lax.Precision.HIGHEST
    real_part = jnp.dot(left[0], right[0], precision=hp) - jnp.dot(left[1], right[1], precision=hp)
    imag_part = jnp.dot(left[0], right[1], precision=hp) + jnp.dot(left[1], right[0], precision=hp)
    return jnp.stack([real_part, imag_part])


def product_transposed(left, right):
    hp = lax.Precision.HIGHEST
    dims = (((1,), (1,)), ((), ()))
    real_part = lax.dot_general(left[0], right[0], dims, precision=hp) - lax.dot_general(left[1], right[1], dims, precision=hp)
    imag_part = lax.dot_general(left[0], right[1], dims, precision=hp) + lax.dot_general(left[1], right[0], dims, precision=hp)
    return jnp.stack([real_part, imag_part])


def reference(trailing, panel, diag_inverse):
    scaled = complex_product(panel, diag_inverse)
    tiles = complex_product(panel[:, :W, :], diag_inverse)
    updated = trailing - product_transposed(panel, tiles)
    return scaled, updated
```

```python
import jax
import jax.numpy as jnp
from jax import lax
from jax.sharding import Mesh
from jax.sharding import PartitionSpec as P

AXES = ("y", "zh", "x", "zl", "core")
ROW = ("y", "zh", "x")
COL = ("zl", "core")


def complex_product(left, right):
    hp = lax.Precision.HIGHEST
    real_part = jnp.dot(left[0], right[0], precision=hp) - jnp.dot(left[1], right[1], precision=hp)
    imag_part = jnp.dot(left[0], right[1], precision=hp) + jnp.dot(left[1], right[0], precision=hp)
    return jnp.stack([real_part, imag_part])


def product_transposed(left, right):
    hp = lax.Precision.HIGHEST
    dims = (((1,), (1,)), ((), ()))
    real_part = lax.dot_general(left[0], right[0], dims, precision=hp) - lax.dot_general(
        left[1], right[1], dims, precision=hp
    )
    imag_part = lax.dot_general(left[0], right[1], dims, precision=hp) + lax.dot_general(
        left[1], right[0], dims, precision=hp
    )
    return jnp.stack([real_part, imag_part])


def make_local(sizes):
    ny, nh, nx, nl, nc = sizes

    def lin(y, h, x, l, c):
        return (((y * nh + h) * nx + x) * nl + l) * nc + c

    pieces = nl * nc
    transpose = []
    for g in range(nx):
        for l in range(nl):
            for c in range(nc):
                p = nc * l + c
                transpose.append((lin(0, 0, g, l, c), lin(0, 0, p % nx, g, p // nx)))

    def shift(y0, y1, h0, h1):
        return [
            (lin(y0, h0, x, l, c), lin(y1, h1, x, l, c))
            for x in range(nx)
            for l in range(nl)
            for c in range(nc)
        ]

    def local(trailing, panel, diag_inverse):
        scaled = complex_product(panel, diag_inverse)
        block = lax.all_gather(panel, COL, axis=1, tiled=True)

        yi = lax.axis_index("y")
        hi = lax.axis_index("zh")
        piece = lax.ppermute(panel, AXES, transpose)
        r1 = lax.ppermute(piece, AXES, shift(0, 1, 0, 0))
        r3 = lax.ppermute(piece, AXES, shift(0, ny - 1, 0, 0))
        r2 = lax.ppermute(r1, AXES, shift(1, 2, 0, 0))
        along_y = jnp.where(yi == 1, r1, jnp.where(yi == 2, r2, jnp.where(yi == ny - 1, r3, piece)))
        rz = lax.ppermute(along_y, AXES, [pr for y in range(ny) for pr in shift(y, y, 0, 1)])
        held = jnp.where(hi == 0, along_y, rz)
        window = lax.all_gather(held, "x", axis=1, tiled=True)

        tiles = complex_product(window, diag_inverse)
        updated = trailing - product_transposed(block, tiles)
        return (scaled, updated)

    return local


def solution(mesh):
    ny, nh, nx = 4, 2, 4
    nl, nc = 4, 2
    devices = mesh.devices.reshape(ny, nh, nx, nl, nc)
    fine = Mesh(devices, AXES)
    return jax.shard_map(
        make_local((ny, nh, nx, nl, nc)),
        mesh=fine,
        in_specs=(P(None, ROW, COL), P(None, ROW + COL, None), P()),
        out_specs=(P(None, ROW + COL, None), P(None, ROW, COL)),
        check_vma=False,
    )
```

```python
import jax
import jax.numpy as jnp
from jax import lax
from jax.sharding import Mesh
from jax.sharding import PartitionSpec as P

AXES = ("y", "zh", "x", "zl", "core")
ROW = ("y", "zh", "x")
COL = ("zl", "core")


def complex_product(left, right):
    hp = lax.Precision.HIGHEST
    real_part = jnp.dot(left[0], right[0], precision=hp) - jnp.dot(left[1], right[1], precision=hp)
    imag_part = jnp.dot(left[0], right[1], precision=hp) + jnp.dot(left[1], right[0], precision=hp)
    return jnp.stack([real_part, imag_part])


def product_transposed(left, right):
    hp = lax.Precision.HIGHEST
    dims = (((1,), (1,)), ((), ()))
    real_part = lax.dot_general(left[0], right[0], dims, precision=hp) - lax.dot_general(
        left[1], right[1], dims, precision=hp
    )
    imag_part = lax.dot_general(left[0], right[1], dims, precision=hp) + lax.dot_general(
        left[1], right[0], dims, precision=hp
    )
    return jnp.stack([real_part, imag_part])


def make_local(sizes):
    ny, nh, nx, nl, nc = sizes

    def lin(y, h, x, l, c):
        return (((y * nh + h) * nx + x) * nl + l) * nc + c

    def plane(h, y):
        return y * nh + h

    def spread(y1, h1):
        pairs = []
        for g in range(nx):
            for l in range(nl):
                for c in range(nc):
                    p = nc * l + c
                    pairs.append((lin(0, 0, g, l, c), lin(y1, h1, p % nx, g, p // nx)))
        return pairs

    first = [(0, 0), (1, 0), (ny - 1, 0), (0, 1)]
    relay_one = [((1, 0), (2, 0)), ((0, 1), (1, 1)), ((ny - 1, 0), (2, 1))]
    relay_two = [((0, 1), (ny - 1, 1))]

    def shifts(n, k):
        return [(i, (i + k) % n) for i in range(n)]

    def reorder(pieces, idx, n):
        out = []
        for j in range(n):
            val = pieces[0]
            for k in range(1, n):
                val = jnp.where((idx - j) % n == k, pieces[k], val)
            out.append(val)
        return jnp.concatenate(out, axis=1)

    def gather(piece, axis, idx, n):
        got = [piece] + [lax.ppermute(piece, axis, shifts(n, k)) for k in range(1, n)]
        return reorder(got, idx, n)

    def local(trailing, panel, diag_inverse):
        scaled = complex_product(panel, diag_inverse)

        yi = lax.axis_index("y")
        hi = lax.axis_index("zh")
        xi = lax.axis_index("x")
        li = lax.axis_index("zl")
        ci = lax.axis_index("core")

        got_a = [lax.ppermute(panel, AXES, spread(y1, h1)) for y1, h1 in first]
        held_a = got_a[0]
        for (y1, h1), got in zip(first[1:], got_a[1:]):
            held_a = jnp.where((yi == y1) & (hi == h1), got, held_a)
        b1 = lax.ppermute(held_a, ("y", "zh"), [(plane(h0, y0), plane(h1, y1)) for (y0, h0), (y1, h1) in relay_one])
        b2 = lax.ppermute(held_a, ("y", "zh"), [(plane(h0, y0), plane(h1, y1)) for (y0, h0), (y1, h1) in relay_two])
        held = held_a
        for (_, _), (y1, h1) in relay_one:
            held = jnp.where((yi == y1) & (hi == h1), b1, held)
        for (_, _), (y1, h1) in relay_two:
            held = jnp.where((yi == y1) & (hi == h1), b2, held)
        window = gather(held, "x", xi, nx)

        mine = gather(panel, "zl", li, nl)
        other = lax.ppermute(mine, "core", shifts(nc, 1))
        lo = jnp.where(ci == 0, mine, other)
        hi_ = jnp.where(ci == 0, other, mine)
        two, rows, width = mine.shape[0], panel.shape[1], mine.shape[2]
        block = jnp.stack(
            [lo.reshape(two, nl, rows, width), hi_.reshape(two, nl, rows, width)], axis=2
        ).reshape(two, nl * nc * rows, width)

        tiles = complex_product(window, diag_inverse)
        updated = trailing - product_transposed(block, tiles)
        return (scaled, updated)

    return local


def solution(mesh):
    ny, nh, nx = 4, 2, 4
    nl, nc = 4, 2
    devices = mesh.devices.reshape(ny, nh, nx, nl, nc)
    fine = Mesh(devices, AXES)
    return jax.shard_map(
        make_local((ny, nh, nx, nl, nc)),
        mesh=fine,
        in_specs=(P(None, ROW, COL), P(None, ROW + COL, None), P()),
        out_specs=(P(None, ROW + COL, None), P(None, ROW, COL)),
        check_vma=False,
    )
```

```python
import jax
import jax.numpy as jnp
from jax import lax
from jax.sharding import Mesh
from jax.sharding import PartitionSpec as P

AXES = ("y", "zh", "x", "zl", "core")
ROW = ("y", "zh", "x")
COL = ("zl", "core")


def complex_product(left, right):
    hp = lax.Precision.HIGHEST
    real_part = jnp.dot(left[0], right[0], precision=hp) - jnp.dot(left[1], right[1], precision=hp)
    imag_part = jnp.dot(left[0], right[1], precision=hp) + jnp.dot(left[1], right[0], precision=hp)
    return jnp.stack([real_part, imag_part])


def product_transposed(left, right):
    hp = lax.Precision.HIGHEST
    dims = (((1,), (1,)), ((), ()))
    real_part = lax.dot_general(left[0], right[0], dims, precision=hp) - lax.dot_general(
        left[1], right[1], dims, precision=hp
    )
    imag_part = lax.dot_general(left[0], right[1], dims, precision=hp) + lax.dot_general(
        left[1], right[0], dims, precision=hp
    )
    return jnp.stack([real_part, imag_part])


def make_local(sizes):
    ny, nh, nx, nl, nc = sizes

    def lin(y, h, x, l, c):
        return (((y * nh + h) * nx + x) * nl + l) * nc + c

    def plane(h, y):
        return y * nh + h

    def spread(y1, h1):
        pairs = []
        for g in range(nx):
            for l in range(nl):
                for c in range(nc):
                    p = nc * l + c
                    pairs.append((lin(0, 0, g, l, c), lin(y1, h1, p % nx, g, p // nx)))
        return pairs

    first = [(0, 0), (1, 0), (ny - 1, 0)]
    relays = [
        [[((1, 0), (2, 0)), ((ny - 1, 0), (ny - 1, 1))], [((1, 0), (1, 1))]],
        [[((1, 1), (2, 1)), ((ny - 1, 1), (0, 1))]],
    ]

    def shifts(n, k):
        return [(i, (i + k) % n) for i in range(n)]

    def reorder(pieces, idx, n):
        out = []
        for j in range(n):
            val = pieces[0]
            for k in range(1, n):
                val = jnp.where((idx - j) % n == k, pieces[k], val)
            out.append(val)
        return jnp.concatenate(out, axis=1)

    def gather(piece, axis, idx, n):
        got = [piece] + [lax.ppermute(piece, axis, shifts(n, k)) for k in range(1, n)]
        return reorder(got, idx, n)

    def local(trailing, panel, diag_inverse):
        scaled = complex_product(panel, diag_inverse)

        yi = lax.axis_index("y")
        hi = lax.axis_index("zh")
        xi = lax.axis_index("x")
        li = lax.axis_index("zl")
        ci = lax.axis_index("core")

        got_a = [lax.ppermute(panel, AXES, spread(y1, h1)) for y1, h1 in first]
        held_a = got_a[0]
        for (y1, h1), got in zip(first[1:], got_a[1:]):
            held_a = jnp.where((yi == y1) & (hi == h1), got, held_a)
        held = held_a
        for stage in relays:
            sent = held
            for pairs in stage:
                got = lax.ppermute(sent, ("y", "zh"), [(plane(h0, y0), plane(h1, y1)) for (y0, h0), (y1, h1) in pairs])
                for _, (y1, h1) in pairs:
                    held = jnp.where((yi == y1) & (hi == h1), got, held)
        window = gather(held, "x", xi, nx)

        mine = gather(panel, "zl", li, nl)
        other = lax.ppermute(mine, "core", shifts(nc, 1))
        lo = jnp.where(ci == 0, mine, other)
        hi_ = jnp.where(ci == 0, other, mine)
        two, rows, width = mine.shape[0], panel.shape[1], mine.shape[2]
        block = jnp.stack(
            [lo.reshape(two, nl, rows, width), hi_.reshape(two, nl, rows, width)], axis=2
        ).reshape(two, nl * nc * rows, width)

        tiles = complex_product(window, diag_inverse)
        updated = trailing - product_transposed(block, tiles)
        return (scaled, updated)

    return local


def solution(mesh):
    ny, nh, nx = 4, 2, 4
    nl, nc = 4, 2
    devices = mesh.devices.reshape(ny, nh, nx, nl, nc)
    fine = Mesh(devices, AXES)
    return jax.shard_map(
        make_local((ny, nh, nx, nl, nc)),
        mesh=fine,
        in_specs=(P(None, ROW, COL), P(None, ROW + COL, None), P()),
        out_specs=(P(None, ROW + COL, None), P(None, ROW, COL)),
        check_vma=False,
    )
```

```python
import jax
import jax.numpy as jnp
from jax import lax
from jax.sharding import Mesh
from jax.sharding import PartitionSpec as P

AXES = ("y", "zh", "x", "zl", "core")
ROW = ("y", "zh", "x")
COL = ("zl", "core")


def complex_product(left, right, hp=lax.Precision.HIGHEST):
    real_part = jnp.dot(left[0], right[0], precision=hp) - jnp.dot(left[1], right[1], precision=hp)
    imag_part = jnp.dot(left[0], right[1], precision=hp) + jnp.dot(left[1], right[0], precision=hp)
    return jnp.stack([real_part, imag_part])


def product_transposed(left, right, hp=lax.Precision.HIGHEST):
    dims = (((1,), (1,)), ((), ()))
    real_part = lax.dot_general(left[0], right[0], dims, precision=hp) - lax.dot_general(
        left[1], right[1], dims, precision=hp
    )
    imag_part = lax.dot_general(left[0], right[1], dims, precision=hp) + lax.dot_general(
        left[1], right[0], dims, precision=hp
    )
    return jnp.stack([real_part, imag_part])


def make_local(sizes):
    ny, nh, nx, nl, nc = sizes

    def lin(y, h, x, l, c):
        return (((y * nh + h) * nx + x) * nl + l) * nc + c

    def plane(h, y):
        return y * nh + h

    def spread(y1, h1):
        pairs = []
        for g in range(nx):
            for l in range(nl):
                for c in range(nc):
                    p = nc * l + c
                    pairs.append((lin(0, 0, g, l, c), lin(y1, h1, p % nx, g, p // nx)))
        return pairs

    first = [(0, 0), (1, 0), (ny - 1, 0)]
    relays = [
        [[((1, 0), (2, 0)), ((ny - 1, 0), (ny - 1, 1))], [((1, 0), (1, 1))]],
        [[((1, 1), (2, 1)), ((ny - 1, 1), (0, 1))]],
    ]

    def shifts(n, k):
        return [(i, (i + k) % n) for i in range(n)]

    def reorder(pieces, idx, n):
        out = []
        for j in range(n):
            val = pieces[0]
            for k in range(1, n):
                val = jnp.where((idx - j) % n == k, pieces[k], val)
            out.append(val)
        return jnp.concatenate(out, axis=1)

    def gather(piece, axis, idx, n):
        got = [piece] + [lax.ppermute(piece, axis, shifts(n, k)) for k in range(1, n)]
        return reorder(got, idx, n)

    def local(trailing, panel, diag_inverse):
        scaled = complex_product(panel, diag_inverse)

        yi = lax.axis_index("y")
        hi = lax.axis_index("zh")
        xi = lax.axis_index("x")
        li = lax.axis_index("zl")
        ci = lax.axis_index("core")

        got_a = [lax.ppermute(panel, AXES, spread(y1, h1)) for y1, h1 in first]
        held_a = got_a[0]
        for (y1, h1), got in zip(first[1:], got_a[1:]):
            held_a = jnp.where((yi == y1) & (hi == h1), got, held_a)
        held = held_a
        for stage in relays:
            sent = held
            for pairs in stage:
                got = lax.ppermute(sent, ("y", "zh"), [(plane(h0, y0), plane(h1, y1)) for (y0, h0), (y1, h1) in pairs])
                for _, (y1, h1) in pairs:
                    held = jnp.where((yi == y1) & (hi == h1), got, held)
        panel_late, held = lax.optimization_barrier((panel, held))
        window = gather(held, "x", xi, nx)

        mine = gather(panel_late, "zl", li, nl)
        other = lax.ppermute(mine, "core", shifts(nc, 1))
        lo = jnp.where(ci == 0, mine, other)
        hi_ = jnp.where(ci == 0, other, mine)
        two, rows, width = mine.shape[0], panel.shape[1], mine.shape[2]
        block = jnp.stack(
            [lo.reshape(two, nl, rows, width), hi_.reshape(two, nl, rows, width)], axis=2
        ).reshape(two, nl * nc * rows, width)

        tiles = complex_product(window, diag_inverse, lax.Precision.HIGH)
        updated = trailing - product_transposed(block, tiles, lax.Precision.HIGH)
        return (scaled, updated)

    return local


def solution(mesh):
    ny, nh, nx = 4, 2, 4
    nl, nc = 4, 2
    devices = mesh.devices.reshape(ny, nh, nx, nl, nc)
    fine = Mesh(devices, AXES)
    return jax.shard_map(
        make_local((ny, nh, nx, nl, nc)),
        mesh=fine,
        in_specs=(P(None, ROW, COL), P(None, ROW + COL, None), P()),
        out_specs=(P(None, ROW + COL, None), P(None, ROW, COL)),
        check_vma=False,
    )
```

```python
import jax
import jax.numpy as jnp
from jax import lax
from jax.sharding import Mesh
from jax.sharding import PartitionSpec as P

AXES = ("y", "zh", "x", "zl", "core")
ROW = ("y", "zh", "x")
COL = ("zl", "core")


def complex_product(left, right, hp=lax.Precision.HIGHEST):
    real_part = jnp.dot(left[0], right[0], precision=hp) - jnp.dot(left[1], right[1], precision=hp)
    imag_part = jnp.dot(left[0], right[1], precision=hp) + jnp.dot(left[1], right[0], precision=hp)
    return jnp.stack([real_part, imag_part])


def product_transposed(left, right, hp=lax.Precision.HIGHEST):
    dims = (((1,), (1,)), ((), ()))
    real_part = lax.dot_general(left[0], right[0], dims, precision=hp) - lax.dot_general(
        left[1], right[1], dims, precision=hp
    )
    imag_part = lax.dot_general(left[0], right[1], dims, precision=hp) + lax.dot_general(
        left[1], right[0], dims, precision=hp
    )
    return jnp.stack([real_part, imag_part])


def make_local(sizes):
    ny, nh, nx, nl, nc = sizes

    def lin(y, h, x, l, c):
        return (((y * nh + h) * nx + x) * nl + l) * nc + c

    def plane(h, y):
        return y * nh + h

    def spread(y1, h1):
        pairs = []
        for g in range(nx):
            for l in range(nl):
                for c in range(nc):
                    p = nc * l + c
                    pairs.append((lin(0, 0, g, l, c), lin(y1, h1, p % nx, g, p // nx)))
        return pairs

    first = [(0, 0), (1, 0), (ny - 1, 0)]
    relays = [
        [[((1, 0), (2, 0)), ((ny - 1, 0), (ny - 1, 1))], [((1, 0), (1, 1))]],
        [[((1, 1), (2, 1)), ((ny - 1, 1), (0, 1))]],
    ]

    def shifts(n, k):
        return [(i, (i + k) % n) for i in range(n)]

    def reorder(pieces, idx, n):
        out = []
        for j in range(n):
            val = pieces[0]
            for k in range(1, n):
                val = jnp.where((idx - j) % n == k, pieces[k], val)
            out.append(val)
        return jnp.concatenate(out, axis=1)

    def gather(piece, axis, idx, n):
        got = [piece] + [lax.ppermute(piece, axis, shifts(n, k)) for k in range(1, n)]
        return reorder(got, idx, n)

    def local(trailing, panel, diag_inverse):
        scaled = complex_product(panel, diag_inverse)

        yi = lax.axis_index("y")
        hi = lax.axis_index("zh")
        xi = lax.axis_index("x")
        li = lax.axis_index("zl")
        ci = lax.axis_index("core")

        got_a = [lax.ppermute(panel, AXES, spread(y1, h1)) for y1, h1 in first]
        held_a = got_a[0]
        for (y1, h1), got in zip(first[1:], got_a[1:]):
            held_a = jnp.where((yi == y1) & (hi == h1), got, held_a)
        held = held_a
        for stage in relays:
            sent = held
            for pairs in stage:
                got = lax.ppermute(sent, ("y", "zh"), [(plane(h0, y0), plane(h1, y1)) for (y0, h0), (y1, h1) in pairs])
                for _, (y1, h1) in pairs:
                    held = jnp.where((yi == y1) & (hi == h1), got, held)
        panel_late, held = lax.optimization_barrier((panel, held))
        window = gather(held, "x", xi, nx)

        mine = gather(panel_late, "zl", li, nl)
        other = lax.ppermute(mine, "core", shifts(nc, 1))
        lo = jnp.where(ci == 0, mine, other)
        hi_ = jnp.where(ci == 0, other, mine)
        two, rows, width = mine.shape[0], panel.shape[1], mine.shape[2]
        block = jnp.stack(
            [lo.reshape(two, nl, rows, width), hi_.reshape(two, nl, rows, width)], axis=2
        ).reshape(two, nl * nc * rows, width)

        tiles = complex_product(window, diag_inverse, lax.Precision.HIGH)
        rhs = jnp.stack([jnp.stack([tiles[0], -tiles[1]]), jnp.stack([tiles[1], tiles[0]])])
        lhs = jnp.broadcast_to(block[None], (rhs.shape[0],) + block.shape)
        dims = (((1, 3), (1, 3)), ((0,), (0,)))
        product = lax.dot_general(lhs, rhs, dims, precision=lax.Precision.HIGH)
        updated = trailing - product
        return (scaled, updated)

    return local


def solution(mesh):
    ny, nh, nx = 4, 2, 4
    nl, nc = 4, 2
    devices = mesh.devices.reshape(ny, nh, nx, nl, nc)
    fine = Mesh(devices, AXES)
    return jax.shard_map(
        make_local((ny, nh, nx, nl, nc)),
        mesh=fine,
        in_specs=(P(None, ROW, COL), P(None, ROW + COL, None), P()),
        out_specs=(P(None, ROW + COL, None), P(None, ROW, COL)),
        check_vma=False,
    )
```

```python
import jax
import jax.numpy as jnp
from jax import lax
from jax.sharding import Mesh
from jax.sharding import PartitionSpec as P

AXES = ("y", "zh", "x", "zl", "core")
ROW = ("y", "zh", "x")
COL = ("zl", "core")


def complex_product(left, right, hp=lax.Precision.HIGHEST):
    real_part = jnp.dot(left[0], right[0], precision=hp) - jnp.dot(left[1], right[1], precision=hp)
    imag_part = jnp.dot(left[0], right[1], precision=hp) + jnp.dot(left[1], right[0], precision=hp)
    return jnp.stack([real_part, imag_part])


def product_transposed(left, right, hp=lax.Precision.HIGHEST):
    dims = (((1,), (1,)), ((), ()))
    real_part = lax.dot_general(left[0], right[0], dims, precision=hp) - lax.dot_general(
        left[1], right[1], dims, precision=hp
    )
    imag_part = lax.dot_general(left[0], right[1], dims, precision=hp) + lax.dot_general(
        left[1], right[0], dims, precision=hp
    )
    return jnp.stack([real_part, imag_part])


def make_local(sizes):
    ny, nh, nx, nl, nc = sizes

    def lin(y, h, x, l, c):
        return (((y * nh + h) * nx + x) * nl + l) * nc + c

    def plane(h, y):
        return y * nh + h

    def spread(y1, h1):
        pairs = []
        for g in range(nx):
            for l in range(nl):
                for c in range(nc):
                    p = nc * l + c
                    pairs.append((lin(0, 0, g, l, c), lin(y1, h1, p % nx, g, p // nx)))
        return pairs

    first = [(0, 0), (1, 0), (ny - 1, 0)]
    relays = [
        [[((1, 0), (2, 0)), ((ny - 1, 0), (ny - 1, 1))], [((1, 0), (1, 1))]],
        [[((1, 1), (2, 1)), ((ny - 1, 1), (0, 1))]],
    ]

    def shifts(n, k):
        return [(i, (i + k) % n) for i in range(n)]

    def reorder(pieces, idx, n):
        out = []
        for j in range(n):
            val = pieces[0]
            for k in range(1, n):
                val = jnp.where((idx - j) % n == k, pieces[k], val)
            out.append(val)
        return jnp.concatenate(out, axis=1)

    def gather(piece, axis, idx, n):
        got = [piece] + [lax.ppermute(piece, axis, shifts(n, k)) for k in range(1, n)]
        return reorder(got, idx, n)

    def local(trailing, panel, diag_inverse):
        scaled = complex_product(panel, diag_inverse)
        block = lax.all_gather(panel, COL, axis=1, tiled=True)

        yi = lax.axis_index("y")
        hi = lax.axis_index("zh")
        xi = lax.axis_index("x")
        li = lax.axis_index("zl")
        ci = lax.axis_index("core")

        got_a = [lax.ppermute(panel, AXES, spread(y1, h1)) for y1, h1 in first]
        held_a = got_a[0]
        for (y1, h1), got in zip(first[1:], got_a[1:]):
            held_a = jnp.where((yi == y1) & (hi == h1), got, held_a)
        held = held_a
        for stage in relays:
            sent = held
            for pairs in stage:
                got = lax.ppermute(sent, ("y", "zh"), [(plane(h0, y0), plane(h1, y1)) for (y0, h0), (y1, h1) in pairs])
                for _, (y1, h1) in pairs:
                    held = jnp.where((yi == y1) & (hi == h1), got, held)
        window = gather(held, "x", xi, nx)


        tiles = complex_product(window, diag_inverse, lax.Precision.HIGH)
        rhs = jnp.stack([jnp.stack([tiles[0], -tiles[1]]), jnp.stack([tiles[1], tiles[0]])])
        lhs = jnp.broadcast_to(block[None], (rhs.shape[0],) + block.shape)
        dims = (((1, 3), (1, 3)), ((0,), (0,)))
        product = lax.dot_general(lhs, rhs, dims, precision=lax.Precision.HIGH)
        updated = trailing - product
        return (scaled, updated)

    return local


def solution(mesh):
    ny, nh, nx = 4, 2, 4
    nl, nc = 4, 2
    devices = mesh.devices.reshape(ny, nh, nx, nl, nc)
    fine = Mesh(devices, AXES)
    return jax.shard_map(
        make_local((ny, nh, nx, nl, nc)),
        mesh=fine,
        in_specs=(P(None, ROW, COL), P(None, ROW + COL, None), P()),
        out_specs=(P(None, ROW + COL, None), P(None, ROW, COL)),
        check_vma=False,
    )
```

```python
import jax
import jax.numpy as jnp
from jax import lax
from jax.sharding import Mesh
from jax.sharding import PartitionSpec as P

AXES = ("y", "zh", "x", "zl", "core")
ROW = ("y", "zh", "x")
COL = ("zl", "core")


def complex_product(left, right, hp=lax.Precision.HIGHEST):
    real_part = jnp.dot(left[0], right[0], precision=hp) - jnp.dot(left[1], right[1], precision=hp)
    imag_part = jnp.dot(left[0], right[1], precision=hp) + jnp.dot(left[1], right[0], precision=hp)
    return jnp.stack([real_part, imag_part])


def product_transposed(left, right, hp=lax.Precision.HIGHEST):
    dims = (((1,), (1,)), ((), ()))
    real_part = lax.dot_general(left[0], right[0], dims, precision=hp) - lax.dot_general(
        left[1], right[1], dims, precision=hp
    )
    imag_part = lax.dot_general(left[0], right[1], dims, precision=hp) + lax.dot_general(
        left[1], right[0], dims, precision=hp
    )
    return jnp.stack([real_part, imag_part])


def make_local(sizes):
    ny, nh, nx, nl, nc = sizes

    def lin(y, h, x, l, c):
        return (((y * nh + h) * nx + x) * nl + l) * nc + c

    def plane(h, y):
        return y * nh + h

    def spread(y1, h1):
        pairs = []
        for g in range(nx):
            for l in range(nl):
                for c in range(nc):
                    p = nc * l + c
                    pairs.append((lin(0, 0, g, l, c), lin(y1, h1, p % nx, g, p // nx)))
        return pairs

    first = [(0, 0), (1, 0), (ny - 1, 0)]
    relays = [
        [[((1, 0), (2, 0)), ((ny - 1, 0), (ny - 1, 1))], [((1, 0), (1, 1))]],
        [[((1, 1), (2, 1)), ((ny - 1, 1), (0, 1))]],
    ]

    def shifts(n, k):
        return [(i, (i + k) % n) for i in range(n)]

    def reorder(pieces, idx, n):
        out = []
        for j in range(n):
            val = pieces[0]
            for k in range(1, n):
                val = jnp.where((idx - j) % n == k, pieces[k], val)
            out.append(val)
        return jnp.concatenate(out, axis=1)

    def gather(piece, axis, idx, n):
        got = [piece] + [lax.ppermute(piece, axis, shifts(n, k)) for k in range(1, n)]
        return reorder(got, idx, n)

    def line_gather(piece, axis, idx, n):
        from_left, from_right = [piece], [piece]
        for d in range(1, n):
            from_left.append(lax.ppermute(from_left[-1], axis, [(i, i + 1) for i in range(d - 1, n - 1)]))
            from_right.append(lax.ppermute(from_right[-1], axis, [(i + 1, i) for i in range(0, n - d)]))
        out = []
        for j in range(n):
            val = piece
            for d in range(1, n):
                val = jnp.where(idx - j == d, from_left[d], val)
                val = jnp.where(j - idx == d, from_right[d], val)
            out.append(val)
        return jnp.concatenate(out, axis=1)

    def local(trailing, panel, diag_inverse):
        scaled = complex_product(panel, diag_inverse)

        yi = lax.axis_index("y")
        hi = lax.axis_index("zh")
        xi = lax.axis_index("x")
        li = lax.axis_index("zl")
        ci = lax.axis_index("core")

        got_a = [lax.ppermute(panel, AXES, spread(y1, h1)) for y1, h1 in first]
        held_a = got_a[0]
        for (y1, h1), got in zip(first[1:], got_a[1:]):
            held_a = jnp.where((yi == y1) & (hi == h1), got, held_a)
        held = held_a
        for stage in relays:
            sent = held
            for pairs in stage:
                got = lax.ppermute(sent, ("y", "zh"), [(plane(h0, y0), plane(h1, y1)) for (y0, h0), (y1, h1) in pairs])
                for _, (y1, h1) in pairs:
                    held = jnp.where((yi == y1) & (hi == h1), got, held)
        panel_late, held = lax.optimization_barrier((panel, held))
        window = gather(held, "x", xi, nx)

        mine = line_gather(panel_late, "zl", li, nl)
        other = lax.ppermute(mine, "core", shifts(nc, 1))
        lo = jnp.where(ci == 0, mine, other)
        hi_ = jnp.where(ci == 0, other, mine)
        two, rows, width = mine.shape[0], panel.shape[1], mine.shape[2]
        block = jnp.stack(
            [lo.reshape(two, nl, rows, width), hi_.reshape(two, nl, rows, width)], axis=2
        ).reshape(two, nl * nc * rows, width)

        tiles = complex_product(window, diag_inverse, lax.Precision.HIGH)
        rhs = jnp.stack([jnp.stack([tiles[0], -tiles[1]]), jnp.stack([tiles[1], tiles[0]])])
        lhs = jnp.broadcast_to(block[None], (rhs.shape[0],) + block.shape)
        dims = (((1, 3), (1, 3)), ((0,), (0,)))
        product = lax.dot_general(lhs, rhs, dims, precision=lax.Precision.HIGH)
        updated = trailing - product
        return (scaled, updated)

    return local


def solution(mesh):
    ny, nh, nx = 4, 2, 4
    nl, nc = 4, 2
    devices = mesh.devices.reshape(ny, nh, nx, nl, nc)
    fine = Mesh(devices, AXES)
    return jax.shard_map(
        make_local((ny, nh, nx, nl, nc)),
        mesh=fine,
        in_specs=(P(None, ROW, COL), P(None, ROW + COL, None), P()),
        out_specs=(P(None, ROW + COL, None), P(None, ROW, COL)),
        check_vma=False,
    )
```

```python
import jax
import jax.numpy as jnp
from jax import lax
from jax.sharding import Mesh
from jax.sharding import PartitionSpec as P

AXES = ("y", "zh", "x", "zl", "core")
ROW = ("y", "zh", "x")
COL = ("zl", "core")


def complex_product(left, right, hp=lax.Precision.HIGHEST):
    real_part = jnp.dot(left[0], right[0], precision=hp) - jnp.dot(left[1], right[1], precision=hp)
    imag_part = jnp.dot(left[0], right[1], precision=hp) + jnp.dot(left[1], right[0], precision=hp)
    return jnp.stack([real_part, imag_part])


def product_transposed(left, right, hp=lax.Precision.HIGHEST):
    dims = (((1,), (1,)), ((), ()))
    real_part = lax.dot_general(left[0], right[0], dims, precision=hp) - lax.dot_general(
        left[1], right[1], dims, precision=hp
    )
    imag_part = lax.dot_general(left[0], right[1], dims, precision=hp) + lax.dot_general(
        left[1], right[0], dims, precision=hp
    )
    return jnp.stack([real_part, imag_part])


def make_local(sizes):
    ny, nh, nx, nl, nc = sizes

    def lin(y, h, x, l, c):
        return (((y * nh + h) * nx + x) * nl + l) * nc + c

    def plane(h, y):
        return y * nh + h

    def spread(y1, h1):
        pairs = []
        for g in range(nx):
            for l in range(nl):
                for c in range(nc):
                    p = nc * l + c
                    pairs.append((lin(0, 0, g, l, c), lin(y1, h1, p % nx, g, p // nx)))
        return pairs

    first = [(0, 0), (1, 0), (ny - 1, 0)]
    relays = [
        [[((1, 0), (2, 0)), ((ny - 1, 0), (ny - 1, 1))], [((1, 0), (1, 1))]],
        [[((1, 1), (2, 1)), ((ny - 1, 1), (0, 1))]],
    ]

    def shifts(n, k):
        return [(i, (i + k) % n) for i in range(n)]

    def reorder(pieces, idx, n):
        out = []
        for j in range(n):
            val = pieces[0]
            for k in range(1, n):
                val = jnp.where((idx - j) % n == k, pieces[k], val)
            out.append(val)
        return jnp.concatenate(out, axis=1)

    def gather(piece, axis, idx, n):
        got = [piece] + [lax.ppermute(piece, axis, shifts(n, k)) for k in range(1, n)]
        return reorder(got, idx, n)

    def local(trailing, panel, diag_inverse):
        scaled = complex_product(panel, diag_inverse)

        yi = lax.axis_index("y")
        hi = lax.axis_index("zh")
        xi = lax.axis_index("x")
        li = lax.axis_index("zl")
        ci = lax.axis_index("core")

        got_a = [lax.ppermute(panel, AXES, spread(y1, h1)) for y1, h1 in first]
        held_a = got_a[0]
        for (y1, h1), got in zip(first[1:], got_a[1:]):
            held_a = jnp.where((yi == y1) & (hi == h1), got, held_a)
        held = held_a
        for stage in relays:
            sent = held
            for pairs in stage:
                got = lax.ppermute(sent, ("y", "zh"), [(plane(h0, y0), plane(h1, y1)) for (y0, h0), (y1, h1) in pairs])
                for _, (y1, h1) in pairs:
                    held = jnp.where((yi == y1) & (hi == h1), got, held)
        window = gather(held, "x", xi, nx)

        mine = gather(panel, "zl", li, nl)
        other = lax.ppermute(mine, "core", shifts(nc, 1))
        lo = jnp.where(ci == 0, mine, other)
        hi_ = jnp.where(ci == 0, other, mine)
        two, rows, width = mine.shape[0], panel.shape[1], mine.shape[2]
        block = jnp.stack(
            [lo.reshape(two, nl, rows, width), hi_.reshape(two, nl, rows, width)], axis=2
        ).reshape(two, nl * nc * rows, width)

        tiles = complex_product(window, diag_inverse, lax.Precision.HIGH)
        rhs = jnp.stack([jnp.stack([tiles[0], -tiles[1]]), jnp.stack([tiles[1], tiles[0]])])
        lhs = jnp.broadcast_to(block[None], (rhs.shape[0],) + block.shape)
        dims = (((1, 3), (1, 3)), ((0,), (0,)))
        product = lax.dot_general(lhs, rhs, dims, precision=lax.Precision.HIGH)
        updated = trailing - product
        return (scaled, updated)

    return local


def solution(mesh):
    ny, nh, nx = 4, 2, 4
    nl, nc = 4, 2
    devices = mesh.devices.reshape(ny, nh, nx, nl, nc)
    fine = Mesh(devices, AXES)
    return jax.shard_map(
        make_local((ny, nh, nx, nl, nc)),
        mesh=fine,
        in_specs=(P(None, ROW, COL), P(None, ROW + COL, None), P()),
        out_specs=(P(None, ROW + COL, None), P(None, ROW, COL)),
        check_vma=False,
    )
```

```python
import jax
import jax.numpy as jnp
from jax import lax
from jax.sharding import Mesh
from jax.sharding import PartitionSpec as P

AXES = ("y", "zh", "x", "zl", "core")
ROW = ("y", "zh", "x")
COL = ("zl", "core")


def complex_product(left, right, hp=lax.Precision.HIGHEST):
    real_part = jnp.dot(left[0], right[0], precision=hp) - jnp.dot(left[1], right[1], precision=hp)
    imag_part = jnp.dot(left[0], right[1], precision=hp) + jnp.dot(left[1], right[0], precision=hp)
    return jnp.stack([real_part, imag_part])


def product_transposed(left, right, hp=lax.Precision.HIGHEST):
    dims = (((1,), (1,)), ((), ()))
    real_part = lax.dot_general(left[0], right[0], dims, precision=hp) - lax.dot_general(
        left[1], right[1], dims, precision=hp
    )
    imag_part = lax.dot_general(left[0], right[1], dims, precision=hp) + lax.dot_general(
        left[1], right[0], dims, precision=hp
    )
    return jnp.stack([real_part, imag_part])


def make_local(sizes):
    ny, nh, nx, nl, nc = sizes

    def lin(y, h, x, l, c):
        return (((y * nh + h) * nx + x) * nl + l) * nc + c

    def plane(h, y):
        return y * nh + h

    def spread(y1, h1):
        pairs = []
        for g in range(nx):
            for l in range(nl):
                for c in range(nc):
                    p = nc * l + c
                    pairs.append((lin(0, 0, g, l, c), lin(y1, h1, p % nx, g, p // nx)))
        return pairs

    first = [(0, 0), (1, 0), (ny - 1, 0)]
    relays = [
        [[((1, 0), (2, 0)), ((ny - 1, 0), (ny - 1, 1))], [((1, 0), (1, 1))]],
        [[((1, 1), (2, 1)), ((ny - 1, 1), (0, 1))]],
    ]

    def shifts(n, k):
        return [(i, (i + k) % n) for i in range(n)]

    def reorder(pieces, idx, n):
        out = []
        for j in range(n):
            val = pieces[0]
            for k in range(1, n):
                val = jnp.where((idx - j) % n == k, pieces[k], val)
            out.append(val)
        return jnp.concatenate(out, axis=1)

    def gather(piece, axis, idx, n):
        got = [piece] + [lax.ppermute(piece, axis, shifts(n, k)) for k in range(1, n)]
        return reorder(got, idx, n)

    def spread_all(piece, axis, n):
        two, rows, width = piece.shape
        copies = jnp.broadcast_to(piece[:, None], (two, n, rows, width))
        got = lax.all_to_all(copies, axis, 1, 1, tiled=True)
        return got.reshape(two, n * rows, width)

    def local(trailing, panel, diag_inverse):
        scaled = complex_product(panel, diag_inverse)

        yi = lax.axis_index("y")
        hi = lax.axis_index("zh")
        xi = lax.axis_index("x")
        li = lax.axis_index("zl")
        ci = lax.axis_index("core")

        got_a = [lax.ppermute(panel, AXES, spread(y1, h1)) for y1, h1 in first]
        held_a = got_a[0]
        for (y1, h1), got in zip(first[1:], got_a[1:]):
            held_a = jnp.where((yi == y1) & (hi == h1), got, held_a)
        held = held_a
        for stage in relays:
            sent = held
            for pairs in stage:
                got = lax.ppermute(sent, ("y", "zh"), [(plane(h0, y0), plane(h1, y1)) for (y0, h0), (y1, h1) in pairs])
                for _, (y1, h1) in pairs:
                    held = jnp.where((yi == y1) & (hi == h1), got, held)
        panel_late, held = lax.optimization_barrier((panel, held))
        window = spread_all(held, "x", nx)

        block = spread_all(panel_late, COL, nl * nc)

        tiles = complex_product(window, diag_inverse, lax.Precision.HIGH)
        rhs = jnp.stack([jnp.stack([tiles[0], -tiles[1]]), jnp.stack([tiles[1], tiles[0]])])
        lhs = jnp.broadcast_to(block[None], (rhs.shape[0],) + block.shape)
        dims = (((1, 3), (1, 3)), ((0,), (0,)))
        product = lax.dot_general(lhs, rhs, dims, precision=lax.Precision.HIGH)
        updated = trailing - product
        return (scaled, updated)

    return local


def solution(mesh):
    ny, nh, nx = 4, 2, 4
    nl, nc = 4, 2
    devices = mesh.devices.reshape(ny, nh, nx, nl, nc)
    fine = Mesh(devices, AXES)
    return jax.shard_map(
        make_local((ny, nh, nx, nl, nc)),
        mesh=fine,
        in_specs=(P(None, ROW, COL), P(None, ROW + COL, None), P()),
        out_specs=(P(None, ROW + COL, None), P(None, ROW, COL)),
        check_vma=False,
    )
```

```python
import jax
import jax.numpy as jnp
from jax import lax
from jax.sharding import Mesh
from jax.sharding import PartitionSpec as P

AXES = ("y", "zh", "x", "zl", "core")
ROW = ("y", "zh", "x")
COL = ("zl", "core")


def complex_product(left, right, hp=lax.Precision.HIGHEST):
    real_part = jnp.dot(left[0], right[0], precision=hp) - jnp.dot(left[1], right[1], precision=hp)
    imag_part = jnp.dot(left[0], right[1], precision=hp) + jnp.dot(left[1], right[0], precision=hp)
    return jnp.stack([real_part, imag_part])


def product_transposed(left, right, hp=lax.Precision.HIGHEST):
    dims = (((1,), (1,)), ((), ()))
    real_part = lax.dot_general(left[0], right[0], dims, precision=hp) - lax.dot_general(
        left[1], right[1], dims, precision=hp
    )
    imag_part = lax.dot_general(left[0], right[1], dims, precision=hp) + lax.dot_general(
        left[1], right[0], dims, precision=hp
    )
    return jnp.stack([real_part, imag_part])


def make_local(sizes):
    ny, nh, nx, nl, nc = sizes

    def lin(y, h, x, l, c):
        return (((y * nh + h) * nx + x) * nl + l) * nc + c

    def plane(h, y):
        return y * nh + h

    def spread(y1, h1):
        pairs = []
        for g in range(nx):
            for l in range(nl):
                for c in range(nc):
                    p = nc * l + c
                    pairs.append((lin(0, 0, g, l, c), lin(y1, h1, p % nx, g, p // nx)))
        return pairs

    first = [(1, 0), (ny - 1, 0)]

    def deal(d):
        pairs = []
        for x in range(nx):
            for l in range(nl):
                for c in range(nc):
                    q = nc * (l % 2) + c
                    pairs.append(((x * nl + l) * nc + c, (((q + d) % nx) * nl + x) * nc + l // 2))
        return pairs
    relays = [
        [[((1, 0), (2, 0)), ((ny - 1, 0), (ny - 1, 1))], [((1, 0), (1, 1))]],
        [[((1, 1), (2, 1)), ((ny - 1, 1), (0, 1))]],
    ]

    def shifts(n, k):
        return [(i, (i + k) % n) for i in range(n)]

    def reorder(pieces, idx, n):
        out = []
        for j in range(n):
            val = pieces[0]
            for k in range(1, n):
                val = jnp.where((idx - j) % n == k, pieces[k], val)
            out.append(val)
        return jnp.concatenate(out, axis=1)

    def gather(piece, axis, idx, n):
        got = [piece] + [lax.ppermute(piece, axis, shifts(n, k)) for k in range(1, n)]
        return reorder(got, idx, n)

    def local(trailing, panel, diag_inverse):
        scaled = complex_product(panel, diag_inverse)

        yi = lax.axis_index("y")
        hi = lax.axis_index("zh")
        xi = lax.axis_index("x")
        li = lax.axis_index("zl")
        ci = lax.axis_index("core")

        held_a = panel
        for y1, h1 in first:
            got = lax.ppermute(panel, ("y", "zh"), [(plane(0, 0), plane(h1, y1))])
            held_a = jnp.where((yi == y1) & (hi == h1), got, held_a)
        held = held_a
        for stage in relays:
            sent = held
            for pairs in stage:
                got = lax.ppermute(sent, ("y", "zh"), [(plane(h0, y0), plane(h1, y1)) for (y0, h0), (y1, h1) in pairs])
                for _, (y1, h1) in pairs:
                    held = jnp.where((yi == y1) & (hi == h1), got, held)
        panel_late, held = lax.optimization_barrier((panel, held))
        dealt = [lax.ppermute(held, ("x", "zl", "core"), deal(d)) for d in range(nx)]
        window = reorder(dealt, xi, nx)

        mine = gather(panel_late, "zl", li, nl)
        other = lax.ppermute(mine, "core", shifts(nc, 1))
        lo = jnp.where(ci == 0, mine, other)
        hi_ = jnp.where(ci == 0, other, mine)
        two, rows, width = mine.shape[0], panel.shape[1], mine.shape[2]
        block = jnp.stack(
            [lo.reshape(two, nl, rows, width), hi_.reshape(two, nl, rows, width)], axis=2
        ).reshape(two, nl * nc * rows, width)

        tiles = complex_product(window, diag_inverse, lax.Precision.HIGH)
        rhs = jnp.stack([jnp.stack([tiles[0], -tiles[1]]), jnp.stack([tiles[1], tiles[0]])])
        lhs = jnp.broadcast_to(block[None], (rhs.shape[0],) + block.shape)
        dims = (((1, 3), (1, 3)), ((0,), (0,)))
        product = lax.dot_general(lhs, rhs, dims, precision=lax.Precision.HIGH)
        updated = trailing - product
        return (scaled, updated)

    return local


def solution(mesh):
    ny, nh, nx = 4, 2, 4
    nl, nc = 4, 2
    devices = mesh.devices.reshape(ny, nh, nx, nl, nc)
    fine = Mesh(devices, AXES)
    return jax.shard_map(
        make_local((ny, nh, nx, nl, nc)),
        mesh=fine,
        in_specs=(P(None, ROW, COL), P(None, ROW + COL, None), P()),
        out_specs=(P(None, ROW + COL, None), P(None, ROW, COL)),
        check_vma=False,
    )
```

```python
import jax
import jax.numpy as jnp
from jax import lax
from jax.sharding import Mesh
from jax.sharding import PartitionSpec as P

AXES = ("y", "zh", "x", "zl", "core")
ROW = ("y", "zh", "x")
COL = ("zl", "core")


def complex_product(left, right, hp=lax.Precision.HIGHEST):
    real_part = jnp.dot(left[0], right[0], precision=hp) - jnp.dot(left[1], right[1], precision=hp)
    imag_part = jnp.dot(left[0], right[1], precision=hp) + jnp.dot(left[1], right[0], precision=hp)
    return jnp.stack([real_part, imag_part])


def product_transposed(left, right, hp=lax.Precision.HIGHEST):
    dims = (((1,), (1,)), ((), ()))
    real_part = lax.dot_general(left[0], right[0], dims, precision=hp) - lax.dot_general(
        left[1], right[1], dims, precision=hp
    )
    imag_part = lax.dot_general(left[0], right[1], dims, precision=hp) + lax.dot_general(
        left[1], right[0], dims, precision=hp
    )
    return jnp.stack([real_part, imag_part])


def permute(value, axis, pairs, parts=2):
    rows = value.shape[1] // parts
    got = [lax.ppermute(value[:, i * rows:(i + 1) * rows], axis, pairs) for i in range(parts)]
    return jnp.concatenate(got, axis=1)


def make_local(sizes):
    ny, nh, nx, nl, nc = sizes

    def lin(y, h, x, l, c):
        return (((y * nh + h) * nx + x) * nl + l) * nc + c

    def plane(h, y):
        return y * nh + h

    def spread(y1, h1):
        pairs = []
        for g in range(nx):
            for l in range(nl):
                for c in range(nc):
                    p = nc * l + c
                    pairs.append((lin(0, 0, g, l, c), lin(y1, h1, p % nx, g, p // nx)))
        return pairs

    first = [(0, 0), (1, 0), (ny - 1, 0)]
    relays = [
        [[((1, 0), (2, 0)), ((ny - 1, 0), (ny - 1, 1))], [((1, 0), (1, 1))]],
        [[((1, 1), (2, 1)), ((ny - 1, 1), (0, 1))]],
    ]

    def shifts(n, k):
        return [(i, (i + k) % n) for i in range(n)]

    def reorder(pieces, idx, n):
        out = []
        for j in range(n):
            val = pieces[0]
            for k in range(1, n):
                val = jnp.where((idx - j) % n == k, pieces[k], val)
            out.append(val)
        return jnp.concatenate(out, axis=1)

    def gather(piece, axis, idx, n):
        got = [piece] + [permute(piece, axis, shifts(n, k)) for k in range(1, n)]
        return reorder(got, idx, n)

    def local(trailing, panel, diag_inverse):
        scaled = complex_product(panel, diag_inverse)

        yi = lax.axis_index("y")
        hi = lax.axis_index("zh")
        xi = lax.axis_index("x")
        li = lax.axis_index("zl")
        ci = lax.axis_index("core")

        got_a = [permute(panel, AXES, spread(y1, h1)) for y1, h1 in first]
        held_a = got_a[0]
        for (y1, h1), got in zip(first[1:], got_a[1:]):
            held_a = jnp.where((yi == y1) & (hi == h1), got, held_a)
        held = held_a
        for stage in relays:
            sent = held
            for pairs in stage:
                got = permute(sent, ("y", "zh"), [(plane(h0, y0), plane(h1, y1)) for (y0, h0), (y1, h1) in pairs])
                for _, (y1, h1) in pairs:
                    held = jnp.where((yi == y1) & (hi == h1), got, held)
        panel_late, held = lax.optimization_barrier((panel, held))
        window = gather(held, "x", xi, nx)

        mine = gather(panel_late, "zl", li, nl)
        other = permute(mine, "core", shifts(nc, 1))
        lo = jnp.where(ci == 0, mine, other)
        hi_ = jnp.where(ci == 0, other, mine)
        two, rows, width = mine.shape[0], panel.shape[1], mine.shape[2]
        block = jnp.stack(
            [lo.reshape(two, nl, rows, width), hi_.reshape(two, nl, rows, width)], axis=2
        ).reshape(two, nl * nc * rows, width)

        tiles = complex_product(window, diag_inverse, lax.Precision.HIGH)
        rhs = jnp.stack([jnp.stack([tiles[0], -tiles[1]]), jnp.stack([tiles[1], tiles[0]])])
        lhs = jnp.broadcast_to(block[None], (rhs.shape[0],) + block.shape)
        dims = (((1, 3), (1, 3)), ((0,), (0,)))
        product = lax.dot_general(lhs, rhs, dims, precision=lax.Precision.HIGH)
        updated = trailing - product
        return (scaled, updated)

    return local


def solution(mesh):
    ny, nh, nx = 4, 2, 4
    nl, nc = 4, 2
    devices = mesh.devices.reshape(ny, nh, nx, nl, nc)
    fine = Mesh(devices, AXES)
    return jax.shard_map(
        make_local((ny, nh, nx, nl, nc)),
        mesh=fine,
        in_specs=(P(None, ROW, COL), P(None, ROW + COL, None), P()),
        out_specs=(P(None, ROW + COL, None), P(None, ROW, COL)),
        check_vma=False,
    )
```

```python
import jax
import jax.numpy as jnp
from jax import lax
from jax.sharding import Mesh
from jax.sharding import PartitionSpec as P

AXES = ("y", "zh", "x", "zl", "core")
ROW = ("y", "zh", "x")
COL = ("zl", "core")


def complex_product(left, right, hp=lax.Precision.HIGHEST):
    real_part = jnp.dot(left[0], right[0], precision=hp) - jnp.dot(left[1], right[1], precision=hp)
    imag_part = jnp.dot(left[0], right[1], precision=hp) + jnp.dot(left[1], right[0], precision=hp)
    return jnp.stack([real_part, imag_part])


def product_transposed(left, right, hp=lax.Precision.HIGHEST):
    dims = (((1,), (1,)), ((), ()))
    real_part = lax.dot_general(left[0], right[0], dims, precision=hp) - lax.dot_general(
        left[1], right[1], dims, precision=hp
    )
    imag_part = lax.dot_general(left[0], right[1], dims, precision=hp) + lax.dot_general(
        left[1], right[0], dims, precision=hp
    )
    return jnp.stack([real_part, imag_part])


def make_local(sizes):
    ny, nh, nx, nl, nc = sizes

    def lin(y, h, x, l, c):
        return (((y * nh + h) * nx + x) * nl + l) * nc + c

    def plane(h, y):
        return y * nh + h

    def spread(y1, h1):
        pairs = []
        for g in range(nx):
            for l in range(nl):
                for c in range(nc):
                    p = nc * l + c
                    pairs.append((lin(0, 0, g, l, c), lin(y1, h1, p % nx, g, p // nx)))
        return pairs

    first = [(0, 0), (1, 0), (ny - 1, 0)]
    relays = [
        [[((1, 0), (2, 0)), ((ny - 1, 0), (ny - 1, 1))]],
        [[((2, 0), (2, 1)), ((ny - 1, 1), (0, 1)), ((1, 0), (1, 1))]],
    ]

    def shifts(n, k):
        return [(i, (i + k) % n) for i in range(n)]

    def reorder(pieces, idx, n):
        out = []
        for j in range(n):
            val = pieces[0]
            for k in range(1, n):
                val = jnp.where((idx - j) % n == k, pieces[k], val)
            out.append(val)
        return jnp.concatenate(out, axis=1)

    def gather(piece, axis, idx, n):
        got = [piece] + [lax.ppermute(piece, axis, shifts(n, k)) for k in range(1, n)]
        return reorder(got, idx, n)

    def local(trailing, panel, diag_inverse):
        scaled = complex_product(panel, diag_inverse)

        yi = lax.axis_index("y")
        hi = lax.axis_index("zh")
        xi = lax.axis_index("x")
        li = lax.axis_index("zl")
        ci = lax.axis_index("core")

        got_a = [lax.ppermute(panel, AXES, spread(y1, h1)) for y1, h1 in first]
        held_a = got_a[0]
        for (y1, h1), got in zip(first[1:], got_a[1:]):
            held_a = jnp.where((yi == y1) & (hi == h1), got, held_a)
        held = held_a
        for stage in relays:
            sent = held
            for pairs in stage:
                got = lax.ppermute(sent, ("y", "zh"), [(plane(h0, y0), plane(h1, y1)) for (y0, h0), (y1, h1) in pairs])
                for _, (y1, h1) in pairs:
                    held = jnp.where((yi == y1) & (hi == h1), got, held)
        panel_late, held = lax.optimization_barrier((panel, held))
        window = gather(held, "x", xi, nx)

        mine = gather(panel_late, "zl", li, nl)
        other = lax.ppermute(mine, "core", shifts(nc, 1))
        lo = jnp.where(ci == 0, mine, other)
        hi_ = jnp.where(ci == 0, other, mine)
        two, rows, width = mine.shape[0], panel.shape[1], mine.shape[2]
        block = jnp.stack(
            [lo.reshape(two, nl, rows, width), hi_.reshape(two, nl, rows, width)], axis=2
        ).reshape(two, nl * nc * rows, width)

        tiles = complex_product(window, diag_inverse, lax.Precision.HIGH)
        rhs = jnp.stack([jnp.stack([tiles[0], -tiles[1]]), jnp.stack([tiles[1], tiles[0]])])
        lhs = jnp.broadcast_to(block[None], (rhs.shape[0],) + block.shape)
        dims = (((1, 3), (1, 3)), ((0,), (0,)))
        product = lax.dot_general(lhs, rhs, dims, precision=lax.Precision.HIGH)
        updated = trailing - product
        return (scaled, updated)

    return local


def solution(mesh):
    ny, nh, nx = 4, 2, 4
    nl, nc = 4, 2
    devices = mesh.devices.reshape(ny, nh, nx, nl, nc)
    fine = Mesh(devices, AXES)
    return jax.shard_map(
        make_local((ny, nh, nx, nl, nc)),
        mesh=fine,
        in_specs=(P(None, ROW, COL), P(None, ROW + COL, None), P()),
        out_specs=(P(None, ROW + COL, None), P(None, ROW, COL)),
        check_vma=False,
    )
```

```python
import jax
import jax.numpy as jnp
from jax import lax
from jax.sharding import Mesh
from jax.sharding import PartitionSpec as P

AXES = ("y", "zh", "x", "zl", "core")
ROW = ("y", "zh", "x")
COL = ("zl", "core")


def complex_product(left, right, hp=lax.Precision.HIGHEST):
    real_part = jnp.dot(left[0], right[0], precision=hp) - jnp.dot(left[1], right[1], precision=hp)
    imag_part = jnp.dot(left[0], right[1], precision=hp) + jnp.dot(left[1], right[0], precision=hp)
    return jnp.stack([real_part, imag_part])


def product_transposed(left, right, hp=lax.Precision.HIGHEST):
    dims = (((1,), (1,)), ((), ()))
    real_part = lax.dot_general(left[0], right[0], dims, precision=hp) - lax.dot_general(
        left[1], right[1], dims, precision=hp
    )
    imag_part = lax.dot_general(left[0], right[1], dims, precision=hp) + lax.dot_general(
        left[1], right[0], dims, precision=hp
    )
    return jnp.stack([real_part, imag_part])


def make_local(sizes):
    ny, nh, nx, nl, nc = sizes

    def lin(y, h, x, l, c):
        return (((y * nh + h) * nx + x) * nl + l) * nc + c

    def plane(h, y):
        return y * nh + h

    def spread(y1, h1):
        pairs = []
        for g in range(nx):
            for l in range(nl):
                for c in range(nc):
                    p = nc * l + c
                    pairs.append((lin(0, 0, g, l, c), lin(y1, h1, p % nx, g, p // nx)))
        return pairs

    first = [(0, 0), (1, 0), (ny - 1, 0)]
    relays = [
        [[((1, 0), (2, 0)), ((ny - 1, 0), (ny - 1, 1))], [((1, 0), (1, 1))]],
        [[((1, 1), (2, 1)), ((ny - 1, 1), (0, 1))]],
    ]

    def shifts(n, k):
        return [(i, (i + k) % n) for i in range(n)]

    def reorder(pieces, idx, n):
        out = []
        for j in range(n):
            val = pieces[0]
            for k in range(1, n):
                val = jnp.where((idx - j) % n == k, pieces[k], val)
            out.append(val)
        return jnp.concatenate(out, axis=1)

    def gather(piece, axis, idx, n):
        got = [piece] + [lax.ppermute(piece, axis, shifts(n, k)) for k in range(1, n)]
        return reorder(got, idx, n)

    def local(trailing, panel, diag_inverse):
        scaled = complex_product(panel, diag_inverse)

        yi = lax.axis_index("y")
        hi = lax.axis_index("zh")
        xi = lax.axis_index("x")
        li = lax.axis_index("zl")
        ci = lax.axis_index("core")

        got_a = [lax.ppermute(panel, AXES, spread(y1, h1)) for y1, h1 in first]
        held_a = got_a[0]
        for (y1, h1), got in zip(first[1:], got_a[1:]):
            held_a = jnp.where((yi == y1) & (hi == h1), got, held_a)
        held = held_a
        for stage in relays:
            sent = held
            for pairs in stage:
                got = lax.ppermute(sent, ("y", "zh"), [(plane(h0, y0), plane(h1, y1)) for (y0, h0), (y1, h1) in pairs])
                for _, (y1, h1) in pairs:
                    held = jnp.where((yi == y1) & (hi == h1), got, held)
        panel_late, held = lax.optimization_barrier((panel, held))
        window = gather(held, "x", xi, nx)
        panel_late, window = lax.optimization_barrier((panel_late, window))

        mine = gather(panel_late, "zl", li, nl)
        other = lax.ppermute(mine, "core", shifts(nc, 1))
        lo = jnp.where(ci == 0, mine, other)
        hi_ = jnp.where(ci == 0, other, mine)
        two, rows, width = mine.shape[0], panel.shape[1], mine.shape[2]
        block = jnp.stack(
            [lo.reshape(two, nl, rows, width), hi_.reshape(two, nl, rows, width)], axis=2
        ).reshape(two, nl * nc * rows, width)

        tiles = complex_product(window, diag_inverse, lax.Precision.HIGH)
        rhs = jnp.stack([jnp.stack([tiles[0], -tiles[1]]), jnp.stack([tiles[1], tiles[0]])])
        lhs = jnp.broadcast_to(block[None], (rhs.shape[0],) + block.shape)
        dims = (((1, 3), (1, 3)), ((0,), (0,)))
        product = lax.dot_general(lhs, rhs, dims, precision=lax.Precision.HIGH)
        updated = trailing - product
        return (scaled, updated)

    return local


def solution(mesh):
    ny, nh, nx = 4, 2, 4
    nl, nc = 4, 2
    devices = mesh.devices.reshape(ny, nh, nx, nl, nc)
    fine = Mesh(devices, AXES)
    return jax.shard_map(
        make_local((ny, nh, nx, nl, nc)),
        mesh=fine,
        in_specs=(P(None, ROW, COL), P(None, ROW + COL, None), P()),
        out_specs=(P(None, ROW + COL, None), P(None, ROW, COL)),
        check_vma=False,
    )
```

```python
import jax
import jax.numpy as jnp
from jax import lax
from jax.sharding import Mesh
from jax.sharding import PartitionSpec as P

AXES = ("y", "zh", "x", "zl", "core")
ROW = ("y", "zh", "x")
COL = ("zl", "core")


def complex_product(left, right, hp=lax.Precision.HIGHEST):
    real_part = jnp.dot(left[0], right[0], precision=hp) - jnp.dot(left[1], right[1], precision=hp)
    imag_part = jnp.dot(left[0], right[1], precision=hp) + jnp.dot(left[1], right[0], precision=hp)
    return jnp.stack([real_part, imag_part])


def product_transposed(left, right, hp=lax.Precision.HIGHEST):
    dims = (((1,), (1,)), ((), ()))
    real_part = lax.dot_general(left[0], right[0], dims, precision=hp) - lax.dot_general(
        left[1], right[1], dims, precision=hp
    )
    imag_part = lax.dot_general(left[0], right[1], dims, precision=hp) + lax.dot_general(
        left[1], right[0], dims, precision=hp
    )
    return jnp.stack([real_part, imag_part])


def make_local(sizes):
    ny, nh, nx, nl, nc = sizes

    def lin(y, h, x, l, c):
        return (((y * nh + h) * nx + x) * nl + l) * nc + c

    def plane(h, y):
        return y * nh + h

    def spread(y1, h1):
        pairs = []
        for g in range(nx):
            for l in range(nl):
                for c in range(nc):
                    p = nc * l + c
                    pairs.append((lin(0, 0, g, l, c), lin(y1, h1, p % nx, g, p // nx)))
        return pairs

    first = [(0, 0), (1, 0), (ny - 1, 0)]
    relays = [
        [[((1, 0), (2, 0)), ((ny - 1, 0), (ny - 1, 1))], [((1, 0), (1, 1))]],
        [[((1, 1), (2, 1)), ((ny - 1, 1), (0, 1))]],
    ]

    def shifts(n, k):
        return [(i, (i + k) % n) for i in range(n)]

    def reorder(pieces, idx, n):
        out = []
        for j in range(n):
            val = pieces[0]
            for k in range(1, n):
                val = jnp.where((idx - j) % n == k, pieces[k], val)
            out.append(val)
        return jnp.concatenate(out, axis=1)

    def gather(piece, axis, idx, n):
        got = [piece] + [lax.ppermute(piece, axis, shifts(n, k)) for k in range(1, n)]
        return reorder(got, idx, n)

    def local(trailing, panel, diag_inverse):
        scaled = complex_product(panel, diag_inverse)

        yi = lax.axis_index("y")
        hi = lax.axis_index("zh")
        xi = lax.axis_index("x")
        li = lax.axis_index("zl")
        ci = lax.axis_index("core")

        got_a = [lax.ppermute(panel, AXES, spread(y1, h1)) for y1, h1 in first]
        held_a = got_a[0]
        for (y1, h1), got in zip(first[1:], got_a[1:]):
            held_a = jnp.where((yi == y1) & (hi == h1), got, held_a)
        held = held_a
        for stage in relays:
            sent = held
            for pairs in stage:
                got = lax.ppermute(sent, ("y", "zh"), [(plane(h0, y0), plane(h1, y1)) for (y0, h0), (y1, h1) in pairs])
                for _, (y1, h1) in pairs:
                    held = jnp.where((yi == y1) & (hi == h1), got, held)
        panel_late, held = lax.optimization_barrier((panel, held))
        window = gather(held, "x", xi, nx)

        got_z = [panel_late] + [lax.ppermute(panel_late, "zl", shifts(nl, k)) for k in range(1, nl)]
        mine = reorder(got_z, li, nl)
        other = reorder([lax.ppermute(g, "core", shifts(nc, 1)) for g in got_z], li, nl)
        lo = jnp.where(ci == 0, mine, other)
        hi_ = jnp.where(ci == 0, other, mine)
        two, rows, width = mine.shape[0], panel.shape[1], mine.shape[2]
        block = jnp.stack(
            [lo.reshape(two, nl, rows, width), hi_.reshape(two, nl, rows, width)], axis=2
        ).reshape(two, nl * nc * rows, width)

        tiles = complex_product(window, diag_inverse, lax.Precision.HIGH)
        rhs = jnp.stack([jnp.stack([tiles[0], -tiles[1]]), jnp.stack([tiles[1], tiles[0]])])
        lhs = jnp.broadcast_to(block[None], (rhs.shape[0],) + block.shape)
        dims = (((1, 3), (1, 3)), ((0,), (0,)))
        product = lax.dot_general(lhs, rhs, dims, precision=lax.Precision.HIGH)
        updated = trailing - product
        return (scaled, updated)

    return local


def solution(mesh):
    ny, nh, nx = 4, 2, 4
    nl, nc = 4, 2
    devices = mesh.devices.reshape(ny, nh, nx, nl, nc)
    fine = Mesh(devices, AXES)
    return jax.shard_map(
        make_local((ny, nh, nx, nl, nc)),
        mesh=fine,
        in_specs=(P(None, ROW, COL), P(None, ROW + COL, None), P()),
        out_specs=(P(None, ROW + COL, None), P(None, ROW, COL)),
        check_vma=False,
    )
```

```python
import jax
import jax.numpy as jnp
from jax import lax
from jax.sharding import Mesh
from jax.sharding import PartitionSpec as P

AXES = ("y", "zh", "x", "zl", "core")
ROW = ("y", "zh", "x")
COL = ("zl", "core")


def complex_product(left, right, hp=lax.Precision.HIGHEST):
    real_part = jnp.dot(left[0], right[0], precision=hp) - jnp.dot(left[1], right[1], precision=hp)
    imag_part = jnp.dot(left[0], right[1], precision=hp) + jnp.dot(left[1], right[0], precision=hp)
    return jnp.stack([real_part, imag_part])


def product_transposed(left, right, hp=lax.Precision.HIGHEST):
    dims = (((1,), (1,)), ((), ()))
    real_part = lax.dot_general(left[0], right[0], dims, precision=hp) - lax.dot_general(
        left[1], right[1], dims, precision=hp
    )
    imag_part = lax.dot_general(left[0], right[1], dims, precision=hp) + lax.dot_general(
        left[1], right[0], dims, precision=hp
    )
    return jnp.stack([real_part, imag_part])


def make_local(sizes):
    ny, nh, nx, nl, nc = sizes

    def lin(y, h, x, l, c):
        return (((y * nh + h) * nx + x) * nl + l) * nc + c

    def plane(h, y):
        return y * nh + h

    def spread(y1, h1):
        pairs = []
        for g in range(nx):
            for l in range(nl):
                for c in range(nc):
                    p = nc * l + c
                    pairs.append((lin(0, 0, g, l, c), lin(y1, h1, p % nx, g, p // nx)))
        return pairs

    first = [(0, 0), (1, 0), (ny - 1, 0), (0, 1)]
    relays = [
        [[((1, 0), (2, 0)), ((0, 1), (1, 1)), ((ny - 1, 0), (2, 1))], [((0, 1), (ny - 1, 1))]],
    ]

    def shifts(n, k):
        return [(i, (i + k) % n) for i in range(n)]

    def reorder(pieces, idx, n):
        out = []
        for j in range(n):
            val = pieces[0]
            for k in range(1, n):
                val = jnp.where((idx - j) % n == k, pieces[k], val)
            out.append(val)
        return jnp.concatenate(out, axis=1)

    def gather(piece, axis, idx, n):
        got = [piece] + [lax.ppermute(piece, axis, shifts(n, k)) for k in range(1, n)]
        return reorder(got, idx, n)

    def local(trailing, panel, diag_inverse):
        scaled = complex_product(panel, diag_inverse)

        yi = lax.axis_index("y")
        hi = lax.axis_index("zh")
        xi = lax.axis_index("x")
        li = lax.axis_index("zl")
        ci = lax.axis_index("core")

        got_a = [lax.ppermute(panel, AXES, spread(y1, h1)) for y1, h1 in first]
        held_a = got_a[0]
        for (y1, h1), got in zip(first[1:], got_a[1:]):
            held_a = jnp.where((yi == y1) & (hi == h1), got, held_a)
        held = held_a
        for stage in relays:
            sent = held
            for pairs in stage:
                got = lax.ppermute(sent, ("y", "zh"), [(plane(h0, y0), plane(h1, y1)) for (y0, h0), (y1, h1) in pairs])
                for _, (y1, h1) in pairs:
                    held = jnp.where((yi == y1) & (hi == h1), got, held)
        panel_late, held = lax.optimization_barrier((panel, held))
        window = gather(held, "x", xi, nx)

        mine = gather(panel_late, "zl", li, nl)
        other = lax.ppermute(mine, "core", shifts(nc, 1))
        lo = jnp.where(ci == 0, mine, other)
        hi_ = jnp.where(ci == 0, other, mine)
        two, rows, width = mine.shape[0], panel.shape[1], mine.shape[2]
        block = jnp.stack(
            [lo.reshape(two, nl, rows, width), hi_.reshape(two, nl, rows, width)], axis=2
        ).reshape(two, nl * nc * rows, width)

        tiles = complex_product(window, diag_inverse, lax.Precision.HIGH)
        rhs = jnp.stack([jnp.stack([tiles[0], -tiles[1]]), jnp.stack([tiles[1], tiles[0]])])
        lhs = jnp.broadcast_to(block[None], (rhs.shape[0],) + block.shape)
        dims = (((1, 3), (1, 3)), ((0,), (0,)))
        product = lax.dot_general(lhs, rhs, dims, precision=lax.Precision.HIGH)
        updated = trailing - product
        return (scaled, updated)

    return local


def solution(mesh):
    ny, nh, nx = 4, 2, 4
    nl, nc = 4, 2
    devices = mesh.devices.reshape(ny, nh, nx, nl, nc)
    fine = Mesh(devices, AXES)
    return jax.shard_map(
        make_local((ny, nh, nx, nl, nc)),
        mesh=fine,
        in_specs=(P(None, ROW, COL), P(None, ROW + COL, None), P()),
        out_specs=(P(None, ROW + COL, None), P(None, ROW, COL)),
        check_vma=False,
    )
```

```python
import jax
import jax.numpy as jnp
from jax import lax
from jax.sharding import Mesh
from jax.sharding import PartitionSpec as P

AXES = ("y", "zh", "x", "zl", "core")
ROW = ("y", "zh", "x")
COL = ("zl", "core")


def complex_product(left, right, hp=lax.Precision.HIGHEST):
    real_part = jnp.dot(left[0], right[0], precision=hp) - jnp.dot(left[1], right[1], precision=hp)
    imag_part = jnp.dot(left[0], right[1], precision=hp) + jnp.dot(left[1], right[0], precision=hp)
    return jnp.stack([real_part, imag_part])


def product_transposed(left, right, hp=lax.Precision.HIGHEST):
    dims = (((1,), (1,)), ((), ()))
    real_part = lax.dot_general(left[0], right[0], dims, precision=hp) - lax.dot_general(
        left[1], right[1], dims, precision=hp
    )
    imag_part = lax.dot_general(left[0], right[1], dims, precision=hp) + lax.dot_general(
        left[1], right[0], dims, precision=hp
    )
    return jnp.stack([real_part, imag_part])


def make_local(sizes):
    ny, nh, nx, nl, nc = sizes

    def lin(y, h, x, l, c):
        return (((y * nh + h) * nx + x) * nl + l) * nc + c

    def plane(h, y):
        return y * nh + h

    def spread(y1, h1):
        pairs = []
        for g in range(nx):
            for l in range(nl):
                for c in range(nc):
                    p = nc * l + c
                    pairs.append((lin(0, 0, g, l, c), lin(y1, h1, p % nx, g, p // nx)))
        return pairs

    first = [(ny - 1, 0), (1, 0), (0, 0)]
    relays = [
        [[((1, 0), (2, 0)), ((ny - 1, 0), (ny - 1, 1))], [((1, 0), (1, 1))]],
        [[((1, 1), (2, 1)), ((ny - 1, 1), (0, 1))]],
    ]

    def shifts(n, k):
        return [(i, (i + k) % n) for i in range(n)]

    def reorder(pieces, idx, n):
        out = []
        for j in range(n):
            val = pieces[0]
            for k in range(1, n):
                val = jnp.where((idx - j) % n == k, pieces[k], val)
            out.append(val)
        return jnp.concatenate(out, axis=1)

    def gather(piece, axis, idx, n):
        got = [piece] + [lax.ppermute(piece, axis, shifts(n, k)) for k in range(1, n)]
        return reorder(got, idx, n)

    def local(trailing, panel, diag_inverse):
        scaled = complex_product(panel, diag_inverse)

        yi = lax.axis_index("y")
        hi = lax.axis_index("zh")
        xi = lax.axis_index("x")
        li = lax.axis_index("zl")
        ci = lax.axis_index("core")

        got_a = [lax.ppermute(panel, AXES, spread(y1, h1)) for y1, h1 in first]
        held_a = got_a[-1]
        for (y1, h1), got in zip(first[:-1], got_a[:-1]):
            held_a = jnp.where((yi == y1) & (hi == h1), got, held_a)
        held = held_a
        for stage in relays:
            sent = held
            for pairs in stage:
                got = lax.ppermute(sent, ("y", "zh"), [(plane(h0, y0), plane(h1, y1)) for (y0, h0), (y1, h1) in pairs])
                for _, (y1, h1) in pairs:
                    held = jnp.where((yi == y1) & (hi == h1), got, held)
        panel_late, held = lax.optimization_barrier((panel, held))
        window = gather(held, "x", xi, nx)

        mine = gather(panel_late, "zl", li, nl)
        other = lax.ppermute(mine, "core", shifts(nc, 1))
        lo = jnp.where(ci == 0, mine, other)
        hi_ = jnp.where(ci == 0, other, mine)
        two, rows, width = mine.shape[0], panel.shape[1], mine.shape[2]
        block = jnp.stack(
            [lo.reshape(two, nl, rows, width), hi_.reshape(two, nl, rows, width)], axis=2
        ).reshape(two, nl * nc * rows, width)

        tiles = complex_product(window, diag_inverse, lax.Precision.HIGH)
        rhs = jnp.stack([jnp.stack([tiles[0], -tiles[1]]), jnp.stack([tiles[1], tiles[0]])])
        lhs = jnp.broadcast_to(block[None], (rhs.shape[0],) + block.shape)
        dims = (((1, 3), (1, 3)), ((0,), (0,)))
        product = lax.dot_general(lhs, rhs, dims, precision=lax.Precision.HIGH)
        updated = trailing - product
        return (scaled, updated)

    return local


def solution(mesh):
    ny, nh, nx = 4, 2, 4
    nl, nc = 4, 2
    devices = mesh.devices.reshape(ny, nh, nx, nl, nc)
    fine = Mesh(devices, AXES)
    return jax.shard_map(
        make_local((ny, nh, nx, nl, nc)),
        mesh=fine,
        in_specs=(P(None, ROW, COL), P(None, ROW + COL, None), P()),
        out_specs=(P(None, ROW + COL, None), P(None, ROW, COL)),
        check_vma=False,
    )
```
